32 devices in a mesh: chain: 2 (over x), ops: 8 (over z, y), sector: 2 (over core).
Axes of the slice: x: 2, y: 2, z: 4, core: 2. Of those that a mesh axis runs over, the one named last changes fastest.
Arguments:
- psi: bfloat16 [2, 8, 384, 384], P('chain', 'sector'), may hold values from -90 to 90
- left_ops: bfloat16 [2, 96, 8, 384, 384], P('chain', 'ops', 'sector'), may hold values from -1 to 2
- right_ops: bfloat16 [2, 96, 8, 384, 384], P('chain', 'ops', 'sector'), may hold values from -1 to 1
- basis: bfloat16 [2, 8, 384, 384], P('chain', 'sector'), may hold values from -0.3125 to 0.3125
- block_dims: int32 [2, 8], P('chain', 'sector'), may hold values from 64 to 384, as said below
Outputs:
- residual: float32 [2, 8, 384, 384], P('chain', 'sector', 'ops')
- thetas: float32 [2, 3], P('chain')
The draws below stay inside these ranges and needn't reach their ends.
Inputs may be any that keep to these rules, and one draw needn't show every extreme that they name: `block_dims`: each is a multiple of 64; every section has a sector of exactly 384.
All inputs are finite; a program needn't handle non-finite values.
Results may differ from the reference program's by a relative error of at most 0.009.
Values may be sent and summed in bfloat16 or wider, within the bound.
No kernel may reach another device: no remote copies, remote signals or barrier semaphores. Data moves between devices by JAX's collectives and lax.ppermute only.
A program may use at most 128 MiB of HBM per device.

```python
import jax
import jax.numpy as jnp
from jax import lax

SECTORS = 8
BLOCK = 384
UNIT = 64
ITERS = 3
SECTIONS = 2
KOPS = 96


def draw_psi(key, part):
    first_key = jax.random.fold_in(key, 0)
    sector_index = jnp.arange(SECTORS, dtype=jnp.float32)
    rising = 3.0 ** (sector_index / max(SECTORS - 1, 1))
    values = jnp.clip(jax.random.normal(first_key, (SECTIONS, SECTORS, BLOCK, BLOCK), jnp.float32), -4.0, 4.0)
    values = values * rising[None, :, None, None]
    return values.astype(jnp.bfloat16)


def operator_draw(key, salt, noise_scale, level):
    random_key = jax.random.fold_in(jax.random.fold_in(key, salt), 0)
    full_shape = (SECTIONS, KOPS, SECTORS, BLOCK, BLOCK)
    eye_block = jnp.eye(BLOCK, dtype=jnp.float32)
    random_part = jnp.clip(jax.random.normal(random_key, full_shape, jnp.float32), -4.0, 4.0)
    levels = jnp.full((SECTIONS, KOPS, 1, 1, 1), level, jnp.float32)
    return random_part * noise_scale + levels * eye_block


def draw_left_ops(key, part):
    return operator_draw(key, 11, float(BLOCK) ** (-0.5), 0.5).astype(jnp.bfloat16)


def draw_right_ops(key, part):
    return operator_draw(key, 13, float(BLOCK * KOPS) ** (-0.5), 2.0 / KOPS).astype(jnp.bfloat16)


def draw_block_dims(key, part):
    first_key, second_key = jax.random.split(jax.random.fold_in(key, 7), 2)
    units = jax.random.randint(first_key, (SECTIONS, SECTORS), 1, BLOCK // UNIT + 1)
    full_sector = jax.random.randint(second_key, (SECTIONS, 1), 0, SECTORS)
    units = jnp.where(jnp.arange(SECTORS)[None, :] == full_sector, BLOCK // UNIT, units)
    return (units * UNIT).astype(jnp.int32)


def shard_levels(rng, shape, cuts, low, high):
    def one(dim, parts):
        draws = jax.random.uniform(jax.random.fold_in(jax.random.fold_in(rng, 6), dim), (parts,), jnp.float32, low / len(cuts), high / len(cuts))
        return jnp.repeat(jnp.exp(draws), shape[dim] // parts).reshape((-1,) + (1,) * (len(shape) - dim - 1))

    gain = one(*cuts[0])
    for cut in cuts[1:]:
        gain = gain * one(*cut)
    return gain


def bell_draw(stream_key, shape, deviation, reach, cuts=(), kind=jnp.bfloat16):
    entries = deviation * jax.random.normal(stream_key, shape, jnp.float32)
    if cuts:
        entries = entries * shard_levels(stream_key, shape, cuts, -0.22, 0.18)
    return jnp.clip(entries, -reach, reach).astype(kind)


def setup_inputs(seed: int = 0) -> dict:
    keys = jax.random.split(jax.random.key(seed), 6)
    psi = draw_psi(jax.random.fold_in(keys[5], 71), 0)
    left_ops = draw_left_ops(jax.random.fold_in(keys[5], 71), 0)
    right_ops = draw_right_ops(jax.random.fold_in(keys[5], 71), 0)
    basis = bell_draw(keys[3], (SECTIONS, SECTORS, BLOCK, BLOCK), BLOCK ** -0.5, 0.3125, ((0, 2), (1, 2)))
    block_dims = draw_block_dims(jax.random.fold_in(keys[5], 71), 0)
    return dict(psi=psi, left_ops=left_ops, right_ops=right_ops, basis=basis, block_dims=block_dims)


def live_mask(block_dims):
    index_rows = jnp.arange(BLOCK, dtype=jnp.int32)
    limits = block_dims[:, :, None, None]
    inside = (index_rows[None, None, :, None] < limits) & (index_rows[None, None, None, :] < limits)
    return inside.astype(jnp.float32)

def reference(psi, left_ops, right_ops, basis, block_dims):
    live = live_mask(block_dims)
    basis_wide = basis.astype(jnp.float32)

    def boundary(index_op):
        left_one = lax.dynamic_index_in_dim(left_ops, index_op, 1, keepdims=False).astype(jnp.float32)
        half_env = jnp.einsum('cqab,cqbd->cqad', left_one, basis_wide)
        half_env = lax.optimization_barrier(half_env.astype(jnp.bfloat16)).astype(jnp.float32)
        return jnp.einsum('cqba,cqbd->cqad', basis_wide, half_env).astype(jnp.bfloat16)
    op_index = jnp.arange(KOPS, dtype=jnp.int32)
    boundary_ops = lax.map(boundary, op_index)
    shifted = jnp.roll(boundary_ops, 1, axis=1)
    vector = jnp.where(live > 0, psi, jnp.zeros_like(psi))
    entry_count = float(SECTORS * BLOCK * BLOCK)
    quotients = []
    residue = jnp.zeros(psi.shape, jnp.float32)
    for iteration in range(ITERS):
        vector_wide = vector.astype(jnp.float32)

        def add_op(total, index_op):
            left_one = shifted[index_op].astype(jnp.float32)
            products = jnp.einsum('cqab,cqbd->cqad', left_one, vector_wide)
            products = lax.optimization_barrier(products.astype(jnp.bfloat16)).astype(jnp.float32)
            right_one = lax.dynamic_index_in_dim(right_ops, index_op, 1, keepdims=False).astype(jnp.float32)
            return (total + jnp.einsum('cqad,cqed->cqae', products, right_one), None)
        sigma_full, _ = lax.scan(add_op, jnp.zeros(psi.shape, jnp.float32), op_index)
        sigma_full = sigma_full * live
        correlation = lax.optimization_barrier(jnp.sum(vector_wide * sigma_full, axis=(1, 2, 3)))
        norm_sum = lax.optimization_barrier(jnp.sum(vector_wide * vector_wide, axis=(1, 2, 3)))
        rayleigh = correlation / norm_sum
        quotients.append(rayleigh)
        residue = sigma_full - rayleigh[:, None, None, None] * vector_wide
        if iteration + 1 < ITERS:
            spread = lax.optimization_barrier(jnp.sum(residue * residue, axis=(1, 2, 3))) / entry_count
            vector = (residue * lax.rsqrt(spread + 1e-06)[:, None, None, None]).astype(jnp.bfloat16)
    return (residue, jnp.stack(quotients, axis=1))
```

```python
import jax
import jax.numpy as jnp
from jax import lax
from jax.sharding import PartitionSpec as P

SECTORS = 8
ITERS = 3


def from_behind(block, axis, distance):
    devices = range(lax.axis_size(axis))
    route = [((i - distance) % len(devices), i) for i in devices]
    return lax.ppermute(block, axis, route)


def live_mask(block_dims, block_size):
    index_rows = jnp.arange(block_size, dtype=jnp.int32)
    limits = block_dims[:, :, None, None]
    inside = (index_rows[None, None, :, None] < limits) & (index_rows[None, None, None, :] < limits)
    return inside.astype(jnp.float32)


def gather_sector(values):
    count = lax.axis_size("sector")
    slots = jnp.zeros((count, values.shape[0]), jnp.float32)
    slots = slots.at[lax.axis_index("sector")].set(values)
    return lax.psum(slots, "sector")


def quotient(vector_wide, sigma_full):
    norm_part = jnp.sum(vector_wide * vector_wide)
    corr_part = jnp.sum(vector_wide * sigma_full)
    local_theta = jnp.where(norm_part > 0, corr_part / jnp.where(norm_part > 0, norm_part, 1.0), 0.0)
    local_rest = sigma_full - local_theta * vector_wide
    rest_part = jnp.sum(local_rest * local_rest)
    cross_part = jnp.sum(vector_wide * local_rest)
    table = gather_sector(jnp.stack([norm_part, corr_part, rest_part, cross_part, local_theta]))
    norms, corrs, rests, crosses, thetas = (table[:, i] for i in range(5))
    rayleigh = jnp.sum(corrs) / jnp.sum(norms)
    shift = thetas - rayleigh
    spread = jnp.sum(rests + 2.0 * shift * crosses + shift * shift * norms)
    return rayleigh, spread


def on_device(psi, left_ops, right_ops, basis, block_dims):
    block_size = psi.shape[2]
    live = live_mask(block_dims, block_size)
    half_env = jnp.einsum(
        "ckqab,cqbd->ckqad", left_ops, basis, preferred_element_type=jnp.float32
    ).astype(jnp.bfloat16)
    boundary_ops = jnp.einsum(
        "cqba,ckqbd->ckqad", basis, half_env, preferred_element_type=jnp.float32
    ).astype(jnp.bfloat16)
    shifted = from_behind(boundary_ops, "chain", 1)
    vector = jnp.where(live > 0, psi, jnp.zeros_like(psi))
    entry_count = float(SECTORS * block_size * block_size)
    share_rows = block_size // lax.axis_size("ops")
    row_start = lax.axis_index("ops") * share_rows
    residual = None
    quotients = []
    for iteration in range(ITERS):
        products = jnp.einsum(
            "ckqab,cqbd->ckqad", shifted, vector, preferred_element_type=jnp.float32
        ).astype(jnp.bfloat16)
        partial_sigma = jnp.einsum(
            "ckqad,ckqed->cqae", products, right_ops, preferred_element_type=jnp.float32
        )
        sigma_full = lax.psum(partial_sigma, "ops") * live
        vector_wide = vector.astype(jnp.float32)
        rayleigh, spread = quotient(vector_wide, sigma_full)
        quotients.append(rayleigh)
        residue = sigma_full - rayleigh * vector_wide
        if iteration + 1 < ITERS:
            vector = (residue * lax.rsqrt(spread / entry_count + 1e-06)).astype(jnp.bfloat16)
        else:
            residual = lax.dynamic_slice_in_dim(residue, row_start, share_rows, 2)
    thetas = jnp.stack(quotients).reshape(1, ITERS)
    return (residual, thetas)


def solution(mesh):
    in_specs = (
        P("chain", "sector", None, None),
        P("chain", "ops", "sector", None, None),
        P("chain", "ops", "sector", None, None),
        P("chain", "sector", None, None),
        P("chain", "sector"),
    )
    out_specs = (P("chain", "sector", "ops", None), P("chain", None))
    return jax.shard_map(
        on_device, mesh=mesh, in_specs=in_specs, out_specs=out_specs, check_vma=False
    )
```

```python
import jax
import jax.numpy as jnp
from jax import lax
from jax.sharding import PartitionSpec as P

SECTORS = 8
ITERS = 3


def from_behind(block, axis, distance):
    devices = range(lax.axis_size(axis))
    route = [((i - distance) % len(devices), i) for i in devices]
    return lax.ppermute(block, axis, route)


def live_mask(block_dims, block_size):
    index_rows = jnp.arange(block_size, dtype=jnp.int32)
    limits = block_dims[:, :, None, None]
    inside = (index_rows[None, None, :, None] < limits) & (index_rows[None, None, None, :] < limits)
    return inside.astype(jnp.float32)

ROW_TILE = 64
LANE_TILE = 128
CLASSES = 8


def tile_counts(dims, block_size):
    rows = jnp.clip((dims + ROW_TILE - 1) // ROW_TILE, 0, block_size // ROW_TILE)
    cols = jnp.clip((dims + LANE_TILE - 1) // LANE_TILE, 0, block_size // LANE_TILE)
    return rows, cols


def tile_plan(dims, block_size):
    rows, cols = tile_counts(dims, block_size)
    row_ids = jnp.arange(block_size // ROW_TILE)[None, :, None]
    col_ids = jnp.arange(block_size // LANE_TILE)[None, None, :]
    needed = ((row_ids < rows[:, None, None]) & (col_ids < cols[:, None, None])).reshape(-1)
    total = needed.shape[0]
    place = jnp.cumsum(needed.astype(jnp.int32)) - 1
    ids = jnp.arange(total, dtype=jnp.int32)
    order = jnp.zeros(total, jnp.int32).at[jnp.where(needed, place, total)].set(ids, mode="drop")
    return order, jnp.sum(needed.astype(jnp.int32))


def size_classes(sectors, block_size):
    total = sectors * (block_size // ROW_TILE) * (block_size // LANE_TILE)
    return sorted({-(-k * total // CLASSES) for k in range(1, CLASSES + 1)})


def tile_index(order, size, block_size):
    per_row = block_size // LANE_TILE
    per_sector = (block_size // ROW_TILE) * per_row
    picked = order[:size]
    return picked // per_sector, (picked // per_row) % (block_size // ROW_TILE), picked % per_row


def tiled(array):
    block_size = array.shape[-1]
    return array.reshape(
        array.shape[:-2] + (block_size // ROW_TILE, ROW_TILE, block_size // LANE_TILE, LANE_TILE)
    )


def pack(array, order, size, lead):
    sector_ids, row_ids, col_ids = tile_index(order, size, array.shape[-1])
    where = (slice(None),) * lead + (sector_ids, row_ids, slice(None), col_ids, slice(None))
    return tiled(array)[where]


def unpack(packed, order, count, size, like, lead):
    sector_ids, row_ids, col_ids = tile_index(order, size, like.shape[-1])
    sector_ids = jnp.where(jnp.arange(size) < count, sector_ids, like.shape[lead])
    where = (slice(None),) * lead + (sector_ids, row_ids, slice(None), col_ids, slice(None))
    room = jnp.zeros(tiled(like).shape, packed.dtype)
    return room.at[where].set(packed, mode="drop").reshape(like.shape)


def class_index(block_dims, block_size, classes):
    every = lax.all_gather(block_dims[0], ("chain", "sector"))
    rows, cols = tile_counts(every, block_size)
    need = jnp.max(jnp.sum(rows * cols, axis=-1))
    return jnp.sum((jnp.asarray(classes, jnp.int32) < need).astype(jnp.int32))


def chain_move(env, send_order, recv_order, recv_count, choice, classes):
    def branch(size):
        def run(env, send_order, recv_order, recv_count):
            arrived = from_behind(pack(env, send_order, size, 2), "chain", 1)
            return unpack(arrived, recv_order, recv_count, size, env, 2)
        return run
    return lax.switch(choice, [branch(s) for s in classes], env, send_order, recv_order, recv_count)


def ops_sum(partial, order, count, choice, classes):
    def branch(size):
        def run(partial, order, count):
            summed = lax.psum(pack(partial, order, size, 1), "ops")
            return unpack(summed, order, count, size, partial, 1)
        return run
    return lax.switch(choice, [branch(s) for s in classes], partial, order, count)


def gather_sector(values):
    count = lax.axis_size("sector")
    slots = jnp.zeros((count, values.shape[0]), jnp.float32)
    slots = slots.at[lax.axis_index("sector")].set(values)
    return lax.psum(slots, "sector")


def quotient(vector_wide, sigma_full):
    norm_part = jnp.sum(vector_wide * vector_wide)
    corr_part = jnp.sum(vector_wide * sigma_full)
    local_theta = jnp.where(norm_part > 0, corr_part / jnp.where(norm_part > 0, norm_part, 1.0), 0.0)
    local_rest = sigma_full - local_theta * vector_wide
    rest_part = jnp.sum(local_rest * local_rest)
    cross_part = jnp.sum(vector_wide * local_rest)
    table = gather_sector(jnp.stack([norm_part, corr_part, rest_part, cross_part, local_theta]))
    norms, corrs, rests, crosses, thetas = (table[:, i] for i in range(5))
    rayleigh = jnp.sum(corrs) / jnp.sum(norms)
    shift = thetas - rayleigh
    spread = jnp.sum(rests + 2.0 * shift * crosses + shift * shift * norms)
    return rayleigh, spread


def on_device(psi, left_ops, right_ops, basis, block_dims):
    block_size = psi.shape[2]
    live = live_mask(block_dims, block_size)
    classes = size_classes(psi.shape[1], block_size)
    choice = class_index(block_dims, block_size, classes)
    own_order, own_count = tile_plan(block_dims[0], block_size)
    target_dims = from_behind(block_dims, "chain", -1)
    send_order, _ = tile_plan(target_dims[0], block_size)
    half_env = jnp.einsum(
        "ckqab,cqbd->ckqad", left_ops, basis, preferred_element_type=jnp.float32
    ).astype(jnp.bfloat16)
    boundary_ops = jnp.einsum(
        "cqba,ckqbd->ckqad", basis, half_env, preferred_element_type=jnp.float32
    ).astype(jnp.bfloat16)
    shifted = chain_move(boundary_ops, send_order, own_order, own_count, choice, classes)
    vector = jnp.where(live > 0, psi, jnp.zeros_like(psi))
    entry_count = float(SECTORS * block_size * block_size)
    share_rows = block_size // lax.axis_size("ops")
    row_start = lax.axis_index("ops") * share_rows
    residual = None
    quotients = []
    for iteration in range(ITERS):
        products = jnp.einsum(
            "ckqab,cqbd->ckqad", shifted, vector, preferred_element_type=jnp.float32
        ).astype(jnp.bfloat16)
        partial_sigma = jnp.einsum(
            "ckqad,ckqed->cqae", products, right_ops, preferred_element_type=jnp.float32
        )
        sigma_full = ops_sum(partial_sigma, own_order, own_count, choice, classes) * live
        vector_wide = vector.astype(jnp.float32)
        rayleigh, spread = quotient(vector_wide, sigma_full)
        quotients.append(rayleigh)
        residue = sigma_full - rayleigh * vector_wide
        if iteration + 1 < ITERS:
            vector = (residue * lax.rsqrt(spread / entry_count + 1e-06)).astype(jnp.bfloat16)
        else:
            residual = lax.dynamic_slice_in_dim(residue, row_start, share_rows, 2)
    thetas = jnp.stack(quotients).reshape(1, ITERS)
    return (residual, thetas)


def solution(mesh):
    in_specs = (
        P("chain", "sector", None, None),
        P("chain", "ops", "sector", None, None),
        P("chain", "ops", "sector", None, None),
        P("chain", "sector", None, None),
        P("chain", "sector"),
    )
    out_specs = (P("chain", "sector", "ops", None), P("chain", None))
    return jax.shard_map(
        on_device, mesh=mesh, in_specs=in_specs, out_specs=out_specs, check_vma=False
    )
```

```python
import jax
import jax.numpy as jnp
from jax import lax
from jax.sharding import PartitionSpec as P

SECTORS = 8
ITERS = 3


def from_behind(block, axis, distance):
    devices = range(lax.axis_size(axis))
    route = [((i - distance) % len(devices), i) for i in devices]
    return lax.ppermute(block, axis, route)


def live_mask(block_dims, block_size):
    index_rows = jnp.arange(block_size, dtype=jnp.int32)
    limits = block_dims[:, :, None, None]
    inside = (index_rows[None, None, :, None] < limits) & (index_rows[None, None, None, :] < limits)
    return inside.astype(jnp.float32)


def ring_order(axis):
    count = lax.axis_size(axis)
    ys = 2
    zs = count // ys
    if count % ys or zs % 2:
        return list(range(count))
    cycle = [z * ys for z in range(zs)]
    for step, z in enumerate(range(zs - 1, -1, -1)):
        cols = range(1, ys) if step % 2 == 0 else range(ys - 1, 0, -1)
        cycle += [z * ys + y for y in cols]
    return cycle


def ring_sum(partial, axis):
    cycle = ring_order(axis)
    count = len(cycle)
    place = jnp.asarray([cycle.index(i) for i in range(count)], jnp.int32)[lax.axis_index(axis)]
    shape = partial.shape
    chunks = partial.reshape(2, count, -1, shape[-1])
    forward = [(cycle[p], cycle[(p + 1) % count]) for p in range(count)]
    backward = [(cycle[p], cycle[(p - 1) % count]) for p in range(count)]
    routes = (forward, backward)
    signs = (1, -1)

    def chunk(half, index):
        return lax.dynamic_index_in_dim(chunks[half], index % count, 0, keepdims=False)

    moving = [chunk(h, place - signs[h]) for h in range(2)]
    for step in range(count - 1):
        for h in range(2):
            arrived = lax.ppermute(moving[h], axis, routes[h])
            moving[h] = arrived + chunk(h, place - signs[h] * (step + 2))
    gathered = []
    for h in range(2):
        table = jnp.zeros(chunks.shape[1:], partial.dtype)
        table = lax.dynamic_update_index_in_dim(table, moving[h], place % count, 0)
        current = moving[h]
        for step in range(count - 1):
            current = lax.ppermute(current, axis, routes[h])
            table = lax.dynamic_update_index_in_dim(
                table, current, (place - signs[h] * (step + 1)) % count, 0
            )
        gathered.append(table)
    return jnp.stack(gathered).reshape(shape)


def gather_sector(values):
    count = lax.axis_size("sector")
    slots = jnp.zeros((count, values.shape[0]), jnp.float32)
    slots = slots.at[lax.axis_index("sector")].set(values)
    return lax.psum(slots, "sector")


def quotient(vector_wide, sigma_full):
    norm_part = jnp.sum(vector_wide * vector_wide)
    corr_part = jnp.sum(vector_wide * sigma_full)
    local_theta = jnp.where(norm_part > 0, corr_part / jnp.where(norm_part > 0, norm_part, 1.0), 0.0)
    local_rest = sigma_full - local_theta * vector_wide
    rest_part = jnp.sum(local_rest * local_rest)
    cross_part = jnp.sum(vector_wide * local_rest)
    table = gather_sector(jnp.stack([norm_part, corr_part, rest_part, cross_part, local_theta]))
    norms, corrs, rests, crosses, thetas = (table[:, i] for i in range(5))
    rayleigh = jnp.sum(corrs) / jnp.sum(norms)
    shift = thetas - rayleigh
    spread = jnp.sum(rests + 2.0 * shift * crosses + shift * shift * norms)
    return rayleigh, spread


def on_device(psi, left_ops, right_ops, basis, block_dims):
    block_size = psi.shape[2]
    live = live_mask(block_dims, block_size)
    half_env = jnp.einsum(
        "ckqab,cqbd->ckqad", left_ops, basis, preferred_element_type=jnp.float32
    ).astype(jnp.bfloat16)
    boundary_ops = jnp.einsum(
        "cqba,ckqbd->ckqad", basis, half_env, preferred_element_type=jnp.float32
    ).astype(jnp.bfloat16)
    shifted = from_behind(boundary_ops, "chain", 1)
    vector = jnp.where(live > 0, psi, jnp.zeros_like(psi))
    entry_count = float(SECTORS * block_size * block_size)
    share_rows = block_size // lax.axis_size("ops")
    row_start = lax.axis_index("ops") * share_rows
    residual = None
    quotients = []
    for iteration in range(ITERS):
        products = jnp.einsum(
            "ckqab,cqbd->ckqad", shifted, vector, preferred_element_type=jnp.float32
        ).astype(jnp.bfloat16)
        partial_sigma = jnp.einsum(
            "ckqad,ckqed->cqae", products, right_ops, preferred_element_type=jnp.float32
        )
        sigma_full = ring_sum(partial_sigma, "ops") * live
        vector_wide = vector.astype(jnp.float32)
        rayleigh, spread = quotient(vector_wide, sigma_full)
        quotients.append(rayleigh)
        residue = sigma_full - rayleigh * vector_wide
        if iteration + 1 < ITERS:
            vector = (residue * lax.rsqrt(spread / entry_count + 1e-06)).astype(jnp.bfloat16)
        else:
            residual = lax.dynamic_slice_in_dim(residue, row_start, share_rows, 2)
    thetas = jnp.stack(quotients).reshape(1, ITERS)
    return (residual, thetas)


def solution(mesh):
    in_specs = (
        P("chain", "sector", None, None),
        P("chain", "ops", "sector", None, None),
        P("chain", "ops", "sector", None, None),
        P("chain", "sector", None, None),
        P("chain", "sector"),
    )
    out_specs = (P("chain", "sector", "ops", None), P("chain", None))
    return jax.shard_map(
        on_device, mesh=mesh, in_specs=in_specs, out_specs=out_specs, check_vma=False
    )
```

```python
import jax
import jax.numpy as jnp
from jax import lax
from jax.sharding import PartitionSpec as P

SECTORS = 8
ITERS = 3


def from_behind(block, axis, distance):
    devices = range(lax.axis_size(axis))
    route = [((i - distance) % len(devices), i) for i in devices]
    return lax.ppermute(block, axis, route)


def live_mask(block_dims, block_size):
    index_rows = jnp.arange(block_size, dtype=jnp.int32)
    limits = block_dims[:, :, None, None]
    inside = (index_rows[None, None, :, None] < limits) & (index_rows[None, None, None, :] < limits)
    return inside.astype(jnp.float32)


def ring_order(axis):
    count = lax.axis_size(axis)
    ys = 2
    zs = count // ys
    if count % ys or zs % 2:
        return list(range(count))
    cycle = [z * ys for z in range(zs)]
    for step, z in enumerate(range(zs - 1, -1, -1)):
        cols = range(1, ys) if step % 2 == 0 else range(ys - 1, 0, -1)
        cycle += [z * ys + y for y in cols]
    return cycle


def ring_sum(partial, axis):
    cycle = ring_order(axis)
    count = len(cycle)
    place = jnp.asarray([cycle.index(i) for i in range(count)], jnp.int32)[lax.axis_index(axis)]
    shape = partial.shape
    chunks = partial.reshape(2, count, -1, shape[-1])
    forward = [(cycle[p], cycle[(p + 1) % count]) for p in range(count)]
    backward = [(cycle[p], cycle[(p - 1) % count]) for p in range(count)]
    routes = (forward, backward)
    signs = (1, -1)

    def chunk(half, index):
        return lax.dynamic_index_in_dim(chunks[half], index % count, 0, keepdims=False)

    moving = [chunk(h, place - signs[h]) for h in range(2)]
    for step in range(count - 1):
        for h in range(2):
            arrived = lax.ppermute(moving[h], axis, routes[h])
            moving[h] = arrived + chunk(h, place - signs[h] * (step + 2))
    gathered = []
    for h in range(2):
        table = jnp.zeros(chunks.shape[1:], partial.dtype)
        table = lax.dynamic_update_index_in_dim(table, moving[h], place % count, 0)
        current = moving[h]
        for step in range(count - 1):
            current = lax.ppermute(current, axis, routes[h])
            table = lax.dynamic_update_index_in_dim(
                table, current, (place - signs[h] * (step + 1)) % count, 0
            )
        gathered.append(table)
    return jnp.stack(gathered).reshape(shape)


ROW_TILE = 64
CLASSES = 8


def row_counts(dims, block_size):
    return jnp.clip((dims + ROW_TILE - 1) // ROW_TILE, 0, block_size // ROW_TILE)


def row_plan(dims, block_size):
    rows = row_counts(dims, block_size)
    needed = (jnp.arange(block_size // ROW_TILE)[None, :] < rows[:, None]).reshape(-1)
    total = needed.shape[0]
    place = jnp.cumsum(needed.astype(jnp.int32)) - 1
    ids = jnp.arange(total, dtype=jnp.int32)
    order = jnp.zeros(total, jnp.int32).at[jnp.where(needed, place, total)].set(ids, mode="drop")
    return order, jnp.sum(rows)


def size_classes(sectors, block_size):
    total = sectors * (block_size // ROW_TILE)
    return sorted({-(-k * total // CLASSES) for k in range(1, CLASSES + 1)})


def class_index(block_dims, block_size, classes):
    every = lax.all_gather(block_dims[0], ("chain", "sector"))
    need = jnp.max(jnp.sum(row_counts(every, block_size), axis=-1))
    return jnp.sum((jnp.asarray(classes, jnp.int32) < need).astype(jnp.int32))


def chain_move(env, send_order, recv_order, recv_count, choice, classes):
    block_size = env.shape[-1]
    ops_here = env.shape[1]
    blocks = env.reshape(ops_here, -1, ROW_TILE, block_size)

    def branch(size):
        def run(blocks, send_order, recv_order, recv_count):
            packed = blocks[:, send_order[:size]]
            arrived = from_behind(packed, "chain", 1)
            slots = jnp.where(jnp.arange(size) < recv_count, recv_order[:size], blocks.shape[1])
            room = jnp.zeros(blocks.shape, blocks.dtype)
            return room.at[:, slots].set(arrived, mode="drop")
        return run
    moved = lax.switch(choice, [branch(s) for s in classes], blocks, send_order, recv_order, recv_count)
    return moved.reshape(env.shape)


def gather_sector(values):
    count = lax.axis_size("sector")
    slots = jnp.zeros((count, values.shape[0]), jnp.float32)
    slots = slots.at[lax.axis_index("sector")].set(values)
    return lax.psum(slots, "sector")


def quotient(vector_wide, sigma_full):
    norm_part = jnp.sum(vector_wide * vector_wide)
    corr_part = jnp.sum(vector_wide * sigma_full)
    local_theta = jnp.where(norm_part > 0, corr_part / jnp.where(norm_part > 0, norm_part, 1.0), 0.0)
    local_rest = sigma_full - local_theta * vector_wide
    rest_part = jnp.sum(local_rest * local_rest)
    cross_part = jnp.sum(vector_wide * local_rest)
    table = gather_sector(jnp.stack([norm_part, corr_part, rest_part, cross_part, local_theta]))
    norms, corrs, rests, crosses, thetas = (table[:, i] for i in range(5))
    rayleigh = jnp.sum(corrs) / jnp.sum(norms)
    shift = thetas - rayleigh
    spread = jnp.sum(rests + 2.0 * shift * crosses + shift * shift * norms)
    return rayleigh, spread


def on_device(psi, left_ops, right_ops, basis, block_dims):
    block_size = psi.shape[2]
    live = live_mask(block_dims, block_size)
    classes = size_classes(psi.shape[1], block_size)
    choice = class_index(block_dims, block_size, classes)
    own_order, own_count = row_plan(block_dims[0], block_size)
    target_dims = from_behind(block_dims, "chain", -1)
    send_order, _ = row_plan(target_dims[0], block_size)
    half_env = jnp.einsum(
        "ckqab,cqbd->ckqad", left_ops, basis, preferred_element_type=jnp.float32
    ).astype(jnp.bfloat16)
    boundary_ops = jnp.einsum(
        "cqba,ckqbd->ckqad", basis, half_env, preferred_element_type=jnp.float32
    ).astype(jnp.bfloat16)
    shifted = chain_move(boundary_ops, send_order, own_order, own_count, choice, classes)
    vector = jnp.where(live > 0, psi, jnp.zeros_like(psi))
    entry_count = float(SECTORS * block_size * block_size)
    share_rows = block_size // lax.axis_size("ops")
    row_start = lax.axis_index("ops") * share_rows
    residual = None
    quotients = []
    for iteration in range(ITERS):
        products = jnp.einsum(
            "ckqab,cqbd->ckqad", shifted, vector, preferred_element_type=jnp.float32
        ).astype(jnp.bfloat16)
        partial_sigma = jnp.einsum(
            "ckqad,ckqed->cqae", products, right_ops, preferred_element_type=jnp.float32
        )
        sigma_full = ring_sum(partial_sigma, "ops") * live
        vector_wide = vector.astype(jnp.float32)
        rayleigh, spread = quotient(vector_wide, sigma_full)
        quotients.append(rayleigh)
        residue = sigma_full - rayleigh * vector_wide
        if iteration + 1 < ITERS:
            vector = (residue * lax.rsqrt(spread / entry_count + 1e-06)).astype(jnp.bfloat16)
        else:
            residual = lax.dynamic_slice_in_dim(residue, row_start, share_rows, 2)
    thetas = jnp.stack(quotients).reshape(1, ITERS)
    return (residual, thetas)


def solution(mesh):
    in_specs = (
        P("chain", "sector", None, None),
        P("chain", "ops", "sector", None, None),
        P("chain", "ops", "sector", None, None),
        P("chain", "sector", None, None),
        P("chain", "sector"),
    )
    out_specs = (P("chain", "sector", "ops", None), P("chain", None))
    return jax.shard_map(
        on_device, mesh=mesh, in_specs=in_specs, out_specs=out_specs, check_vma=False
    )
```

```python
import jax
import jax.numpy as jnp
from jax import lax
from jax.sharding import PartitionSpec as P

SECTORS = 8
ITERS = 3


def from_behind(block, axis, distance):
    devices = range(lax.axis_size(axis))
    route = [((i - distance) % len(devices), i) for i in devices]
    return lax.ppermute(block, axis, route)


def live_mask(block_dims, block_size):
    index_rows = jnp.arange(block_size, dtype=jnp.int32)
    limits = block_dims[:, :, None, None]
    inside = (index_rows[None, None, :, None] < limits) & (index_rows[None, None, None, :] < limits)
    return inside.astype(jnp.float32)


def ring_order(axis):
    count = lax.axis_size(axis)
    ys = 2
    zs = count // ys
    if count % ys or zs % 2:
        return list(range(count))
    cycle = [z * ys for z in range(zs)]
    for step, z in enumerate(range(zs - 1, -1, -1)):
        cols = range(1, ys) if step % 2 == 0 else range(ys - 1, 0, -1)
        cycle += [z * ys + y for y in cols]
    return cycle


def ring_sum(partial, axis):
    cycle = ring_order(axis)
    count = len(cycle)
    place = jnp.asarray([cycle.index(i) for i in range(count)], jnp.int32)[lax.axis_index(axis)]
    shape = partial.shape
    chunks = partial.reshape(2, count, -1, shape[-1])
    forward = [(cycle[p], cycle[(p + 1) % count]) for p in range(count)]
    backward = [(cycle[p], cycle[(p - 1) % count]) for p in range(count)]
    routes = (forward, backward)
    signs = (1, -1)

    def chunk(half, index):
        return lax.dynamic_index_in_dim(chunks[half], index % count, 0, keepdims=False)

    moving = [chunk(h, place - signs[h]) for h in range(2)]
    for step in range(count - 1):
        for h in range(2):
            arrived = lax.ppermute(moving[h], axis, routes[h])
            moving[h] = arrived + chunk(h, place - signs[h] * (step + 2))
    gathered = []
    for h in range(2):
        table = jnp.zeros(chunks.shape[1:], partial.dtype)
        table = lax.dynamic_update_index_in_dim(table, moving[h], place % count, 0)
        current = moving[h]
        for step in range(count - 1):
            current = lax.ppermute(current, axis, routes[h])
            table = lax.dynamic_update_index_in_dim(
                table, current, (place - signs[h] * (step + 1)) % count, 0
            )
        gathered.append(table)
    return jnp.stack(gathered).reshape(shape)


def gather_sector(values):
    count = lax.axis_size("sector")
    slots = jnp.zeros((count, values.shape[0]), jnp.float32)
    slots = slots.at[lax.axis_index("sector")].set(values)
    return lax.psum(slots, "sector")


def quotient(vector_wide, sigma_full):
    norm_part = jnp.sum(vector_wide * vector_wide)
    corr_part = jnp.sum(vector_wide * sigma_full)
    local_theta = jnp.where(norm_part > 0, corr_part / jnp.where(norm_part > 0, norm_part, 1.0), 0.0)
    local_rest = sigma_full - local_theta * vector_wide
    rest_part = jnp.sum(local_rest * local_rest)
    cross_part = jnp.sum(vector_wide * local_rest)
    table = gather_sector(jnp.stack([norm_part, corr_part, rest_part, cross_part, local_theta]))
    norms, corrs, rests, crosses, thetas = (table[:, i] for i in range(5))
    rayleigh = jnp.sum(corrs) / jnp.sum(norms)
    shift = thetas - rayleigh
    spread = jnp.sum(rests + 2.0 * shift * crosses + shift * shift * norms)
    return rayleigh, spread


def on_device(psi, left_ops, right_ops, basis, block_dims):
    block_size = psi.shape[2]
    live = live_mask(block_dims, block_size)
    ops_here = left_ops.shape[1]
    pieces = 3 if ops_here % 3 == 0 else (2 if ops_here % 2 == 0 else 1)
    width = ops_here // pieces
    spans = [slice(i * width, (i + 1) * width) for i in range(pieces)]
    shifted = []
    for span in spans:
        half_env = jnp.einsum(
            "ckqab,cqbd->ckqad", left_ops[:, span], basis, preferred_element_type=jnp.float32
        ).astype(jnp.bfloat16)
        boundary_ops = jnp.einsum(
            "cqba,ckqbd->ckqad", basis, half_env, preferred_element_type=jnp.float32
        ).astype(jnp.bfloat16)
        shifted.append(from_behind(boundary_ops, "chain", 1))
    vector = jnp.where(live > 0, psi, jnp.zeros_like(psi))
    entry_count = float(SECTORS * block_size * block_size)
    share_rows = block_size // lax.axis_size("ops")
    row_start = lax.axis_index("ops") * share_rows
    residual = None
    quotients = []
    for iteration in range(ITERS):
        partial_sigma = None
        for span, moved in zip(spans, shifted):
            products = jnp.einsum(
                "ckqab,cqbd->ckqad", moved, vector, preferred_element_type=jnp.float32
            ).astype(jnp.bfloat16)
            term = jnp.einsum(
                "ckqad,ckqed->cqae", products, right_ops[:, span], preferred_element_type=jnp.float32
            )
            partial_sigma = term if partial_sigma is None else partial_sigma + term
        sigma_full = ring_sum(partial_sigma, "ops") * live
        vector_wide = vector.astype(jnp.float32)
        rayleigh, spread = quotient(vector_wide, sigma_full)
        quotients.append(rayleigh)
        residue = sigma_full - rayleigh * vector_wide
        if iteration + 1 < ITERS:
            vector = (residue * lax.rsqrt(spread / entry_count + 1e-06)).astype(jnp.bfloat16)
        else:
            residual = lax.dynamic_slice_in_dim(residue, row_start, share_rows, 2)
    thetas = jnp.stack(quotients).reshape(1, ITERS)
    return (residual, thetas)


def solution(mesh):
    in_specs = (
        P("chain", "sector", None, None),
        P("chain", "ops", "sector", None, None),
        P("chain", "ops", "sector", None, None),
        P("chain", "sector", None, None),
        P("chain", "sector"),
    )
    out_specs = (P("chain", "sector", "ops", None), P("chain", None))
    return jax.shard_map(
        on_device, mesh=mesh, in_specs=in_specs, out_specs=out_specs, check_vma=False
    )
```

```python
import jax
import jax.numpy as jnp
from jax import lax
from jax.sharding import PartitionSpec as P

SECTORS = 8
ITERS = 3


def from_behind(block, axis, distance):
    devices = range(lax.axis_size(axis))
    route = [((i - distance) % len(devices), i) for i in devices]
    return lax.ppermute(block, axis, route)


def live_mask(block_dims, block_size):
    index_rows = jnp.arange(block_size, dtype=jnp.int32)
    limits = block_dims[:, :, None, None]
    inside = (index_rows[None, None, :, None] < limits) & (index_rows[None, None, None, :] < limits)
    return inside.astype(jnp.float32)


def ring_order(axis):
    count = lax.axis_size(axis)
    ys = 2
    zs = count // ys
    if count % ys or zs % 2:
        return list(range(count))
    cycle = [z * ys for z in range(zs)]
    for step, z in enumerate(range(zs - 1, -1, -1)):
        cols = range(1, ys) if step % 2 == 0 else range(ys - 1, 0, -1)
        cycle += [z * ys + y for y in cols]
    return cycle


def ring_sum(partial, axis):
    cycle = ring_order(axis)
    count = len(cycle)
    place = jnp.asarray([cycle.index(i) for i in range(count)], jnp.int32)[lax.axis_index(axis)]
    shape = partial.shape
    chunks = partial.reshape(2, count, -1, shape[-1])
    forward = [(cycle[p], cycle[(p + 1) % count]) for p in range(count)]
    backward = [(cycle[p], cycle[(p - 1) % count]) for p in range(count)]
    routes = (forward, backward)
    signs = (1, -1)

    def chunk(half, index):
        return lax.dynamic_index_in_dim(chunks[half], index % count, 0, keepdims=False)

    moving = [chunk(h, place - signs[h]) for h in range(2)]
    for step in range(count - 1):
        for h in range(2):
            arrived = lax.ppermute(moving[h], axis, routes[h])
            moving[h] = arrived + chunk(h, place - signs[h] * (step + 2))
    gathered = []
    for h in range(2):
        table = jnp.zeros(chunks.shape[1:], partial.dtype)
        table = lax.dynamic_update_index_in_dim(table, moving[h], place % count, 0)
        current = moving[h]
        for step in range(count - 1):
            current = lax.ppermute(current, axis, routes[h])
            table = lax.dynamic_update_index_in_dim(
                table, current, (place - signs[h] * (step + 1)) % count, 0
            )
        gathered.append(table)
    return jnp.stack(gathered).reshape(shape)


def ring_sigma(moved, vector, right_ops, axis):
    cycle = ring_order(axis)
    count = len(cycle)
    place = jnp.asarray([cycle.index(i) for i in range(count)], jnp.int32)[lax.axis_index(axis)]
    _, ops_here, sectors, block_size, _ = moved.shape
    rows = sectors * block_size // (2 * count)
    forward = [(cycle[p], cycle[(p + 1) % count]) for p in range(count)]
    backward = [(cycle[p], cycle[(p - 1) % count]) for p in range(count)]
    routes = (forward, backward)
    signs = (1, -1)

    def chunk(half, index):
        start = (half * count + index % count) * rows
        sector, row = start // block_size, start % block_size
        left = lax.dynamic_slice(moved, (0, 0, sector, row, 0), (1, ops_here, 1, rows, block_size))
        vec = lax.dynamic_slice(vector, (0, sector, 0, 0), (1, 1, block_size, block_size))
        right = lax.dynamic_slice(right_ops, (0, 0, sector, 0, 0), (1, ops_here, 1, block_size, block_size))
        products = jnp.einsum(
            "ckqab,cqbd->ckqad", left, vec, preferred_element_type=jnp.float32
        ).astype(jnp.bfloat16)
        return jnp.einsum(
            "ckqad,ckqed->cqae", products, right, preferred_element_type=jnp.float32
        ).reshape(rows, block_size)

    moving = [chunk(h, place - signs[h]) for h in range(2)]
    for step in range(count - 1):
        for h in range(2):
            arrived = lax.ppermute(moving[h], axis, routes[h])
            moving[h] = arrived + chunk(h, place - signs[h] * (step + 2))
    gathered = []
    for h in range(2):
        table = jnp.zeros((count, rows, block_size), jnp.float32)
        table = lax.dynamic_update_index_in_dim(table, moving[h], place % count, 0)
        current = moving[h]
        for step in range(count - 1):
            current = lax.ppermute(current, axis, routes[h])
            table = lax.dynamic_update_index_in_dim(
                table, current, (place - signs[h] * (step + 1)) % count, 0
            )
        gathered.append(table)
    return jnp.stack(gathered).reshape(1, sectors, block_size, block_size)


def gather_sector(values):
    count = lax.axis_size("sector")
    slots = jnp.zeros((count, values.shape[0]), jnp.float32)
    slots = slots.at[lax.axis_index("sector")].set(values)
    return lax.psum(slots, "sector")


def quotient(vector_wide, sigma_full):
    norm_part = jnp.sum(vector_wide * vector_wide)
    corr_part = jnp.sum(vector_wide * sigma_full)
    local_theta = jnp.where(norm_part > 0, corr_part / jnp.where(norm_part > 0, norm_part, 1.0), 0.0)
    local_rest = sigma_full - local_theta * vector_wide
    rest_part = jnp.sum(local_rest * local_rest)
    cross_part = jnp.sum(vector_wide * local_rest)
    table = gather_sector(jnp.stack([norm_part, corr_part, rest_part, cross_part, local_theta]))
    norms, corrs, rests, crosses, thetas = (table[:, i] for i in range(5))
    rayleigh = jnp.sum(corrs) / jnp.sum(norms)
    shift = thetas - rayleigh
    spread = jnp.sum(rests + 2.0 * shift * crosses + shift * shift * norms)
    return rayleigh, spread


def on_device(psi, left_ops, right_ops, basis, block_dims):
    block_size = psi.shape[2]
    live = live_mask(block_dims, block_size)
    half_env = jnp.einsum(
        "ckqab,cqbd->ckqad", left_ops, basis, preferred_element_type=jnp.float32
    ).astype(jnp.bfloat16)
    boundary_ops = jnp.einsum(
        "cqba,ckqbd->ckqad", basis, half_env, preferred_element_type=jnp.float32
    ).astype(jnp.bfloat16)
    shifted = from_behind(boundary_ops, "chain", 1)
    vector = jnp.where(live > 0, psi, jnp.zeros_like(psi))
    entry_count = float(SECTORS * block_size * block_size)
    share_rows = block_size // lax.axis_size("ops")
    row_start = lax.axis_index("ops") * share_rows
    residual = None
    quotients = []
    for iteration in range(ITERS):
        sigma_full = ring_sigma(shifted, vector, right_ops, "ops") * live
        vector_wide = vector.astype(jnp.float32)
        rayleigh, spread = quotient(vector_wide, sigma_full)
        quotients.append(rayleigh)
        residue = sigma_full - rayleigh * vector_wide
        if iteration + 1 < ITERS:
            vector = (residue * lax.rsqrt(spread / entry_count + 1e-06)).astype(jnp.bfloat16)
        else:
            residual = lax.dynamic_slice_in_dim(residue, row_start, share_rows, 2)
    thetas = jnp.stack(quotients).reshape(1, ITERS)
    return (residual, thetas)


def solution(mesh):
    in_specs = (
        P("chain", "sector", None, None),
        P("chain", "ops", "sector", None, None),
        P("chain", "ops", "sector", None, None),
        P("chain", "sector", None, None),
        P("chain", "sector"),
    )
    out_specs = (P("chain", "sector", "ops", None), P("chain", None))
    return jax.shard_map(
        on_device, mesh=mesh, in_specs=in_specs, out_specs=out_specs, check_vma=False
    )
```

```python
import jax
import jax.numpy as jnp
from jax import lax
from jax.sharding import PartitionSpec as P

SECTORS = 8
ITERS = 3


def from_behind(block, axis, distance):
    devices = range(lax.axis_size(axis))
    route = [((i - distance) % len(devices), i) for i in devices]
    return lax.ppermute(block, axis, route)


def live_mask(block_dims, block_size):
    index_rows = jnp.arange(block_size, dtype=jnp.int32)
    limits = block_dims[:, :, None, None]
    inside = (index_rows[None, None, :, None] < limits) & (index_rows[None, None, None, :] < limits)
    return inside.astype(jnp.float32)


def ring_order(axis):
    count = lax.axis_size(axis)
    ys = 2
    zs = count // ys
    if count % ys or zs % 2:
        return list(range(count))
    cycle = [z * ys for z in range(zs)]
    for step, z in enumerate(range(zs - 1, -1, -1)):
        cols = range(1, ys) if step % 2 == 0 else range(ys - 1, 0, -1)
        cycle += [z * ys + y for y in cols]
    return cycle


def ring_sum(partial, axis):
    cycle = ring_order(axis)
    count = len(cycle)
    place = jnp.asarray([cycle.index(i) for i in range(count)], jnp.int32)[lax.axis_index(axis)]
    shape = partial.shape
    chunks = partial.reshape(2, count, -1, shape[-1])
    forward = [(cycle[p], cycle[(p + 1) % count]) for p in range(count)]
    backward = [(cycle[p], cycle[(p - 1) % count]) for p in range(count)]
    routes = (forward, backward)
    signs = (1, -1)

    def chunk(half, index):
        return lax.dynamic_index_in_dim(chunks[half], index % count, 0, keepdims=False)

    moving = [chunk(h, place - signs[h]) for h in range(2)]
    for step in range(count - 1):
        for h in range(2):
            arrived = lax.ppermute(moving[h], axis, routes[h])
            moving[h] = arrived + chunk(h, place - signs[h] * (step + 2))
    gathered = []
    for h in range(2):
        table = jnp.zeros(chunks.shape[1:], partial.dtype)
        table = lax.dynamic_update_index_in_dim(table, moving[h], place % count, 0)
        current = moving[h]
        for step in range(count - 1):
            current = lax.ppermute(current, axis, routes[h])
            table = lax.dynamic_update_index_in_dim(
                table, current, (place - signs[h] * (step + 1)) % count, 0
            )
        gathered.append(table)
    return jnp.stack(gathered).reshape(shape)


def gather_sector(values):
    count = lax.axis_size("sector")
    mine = jnp.arange(count)[:, None] == lax.axis_index("sector")
    return lax.psum(jnp.where(mine, values[None, :], 0.0), "sector")


def quotient(vector_wide, sigma_full):
    norm_part = jnp.sum(vector_wide * vector_wide)
    corr_part = jnp.sum(vector_wide * sigma_full)
    local_theta = jnp.where(norm_part > 0, corr_part / jnp.where(norm_part > 0, norm_part, 1.0), 0.0)
    local_rest = sigma_full - local_theta * vector_wide
    rest_part = jnp.sum(local_rest * local_rest)
    cross_part = jnp.sum(vector_wide * local_rest)
    table = gather_sector(jnp.stack([norm_part, corr_part, rest_part, cross_part, local_theta]))
    norms, corrs, rests, crosses, thetas = (table[:, i] for i in range(5))
    rayleigh = jnp.sum(corrs) / jnp.sum(norms)
    shift = thetas - rayleigh
    spread = jnp.sum(rests + 2.0 * shift * crosses + shift * shift * norms)
    return rayleigh, spread


def on_device(psi, left_ops, right_ops, basis, block_dims):
    block_size = psi.shape[2]
    live = live_mask(block_dims, block_size)
    half_env = jnp.einsum(
        "ckqab,cqbd->ckqad", left_ops, basis, preferred_element_type=jnp.float32
    ).astype(jnp.bfloat16)
    boundary_ops = jnp.einsum(
        "cqba,ckqbd->ckqad", basis, half_env, preferred_element_type=jnp.float32
    ).astype(jnp.bfloat16)
    shifted = from_behind(boundary_ops, "chain", 1)
    vector = jnp.where(live > 0, psi, jnp.zeros_like(psi))
    entry_count = float(SECTORS * block_size * block_size)
    share_rows = block_size // lax.axis_size("ops")
    row_start = lax.axis_index("ops") * share_rows
    residual = None
    quotients = []
    for iteration in range(ITERS):
        products = jnp.einsum(
            "ckqab,cqbd->ckqad", shifted, vector, preferred_element_type=jnp.float32
        ).astype(jnp.bfloat16)
        partial_sigma = jnp.einsum(
            "ckqad,ckqed->cqae", products, right_ops, preferred_element_type=jnp.float32
        )
        sigma_full = ring_sum(partial_sigma, "ops") * live
        vector_wide = vector.astype(jnp.float32)
        rayleigh, spread = quotient(vector_wide, sigma_full)
        quotients.append(rayleigh)
        residue = sigma_full - rayleigh * vector_wide
        if iteration + 1 < ITERS:
            vector = (residue * lax.rsqrt(spread / entry_count + 1e-06)).astype(jnp.bfloat16)
        else:
            residual = lax.dynamic_slice_in_dim(residue, row_start, share_rows, 2)
    thetas = jnp.stack(quotients).reshape(1, ITERS)
    return (residual, thetas)


def solution(mesh):
    in_specs = (
        P("chain", "sector", None, None),
        P("chain", "ops", "sector", None, None),
        P("chain", "ops", "sector", None, None),
        P("chain", "sector", None, None),
        P("chain", "sector"),
    )
    out_specs = (P("chain", "sector", "ops", None), P("chain", None))
    return jax.shard_map(
        on_device, mesh=mesh, in_specs=in_specs, out_specs=out_specs, check_vma=False
    )
```

```python
import jax
import jax.numpy as jnp
from jax import lax
from jax.sharding import PartitionSpec as P

SECTORS = 8
ITERS = 3


def from_behind(block, axis, distance):
    devices = range(lax.axis_size(axis))
    route = [((i - distance) % len(devices), i) for i in devices]
    return lax.ppermute(block, axis, route)


def live_mask(block_dims, block_size):
    index_rows = jnp.arange(block_size, dtype=jnp.int32)
    limits = block_dims[:, :, None, None]
    inside = (index_rows[None, None, :, None] < limits) & (index_rows[None, None, None, :] < limits)
    return inside.astype(jnp.float32)


def ring_order(axis):
    count = lax.axis_size(axis)
    ys = 2
    zs = count // ys
    if count % ys or zs % 2:
        return list(range(count))
    cycle = [z * ys for z in range(zs)]
    for step, z in enumerate(range(zs - 1, -1, -1)):
        cols = range(1, ys) if step % 2 == 0 else range(ys - 1, 0, -1)
        cycle += [z * ys + y for y in cols]
    return cycle


def ring_sum(partial, axis, gather=True):
    cycle = ring_order(axis)
    count = len(cycle)
    place = jnp.asarray([cycle.index(i) for i in range(count)], jnp.int32)[lax.axis_index(axis)]
    ids = jnp.asarray(cycle, jnp.int32)
    _, sectors, block_size, _ = partial.shape
    rows = block_size // (2 * count)
    blocks = partial.reshape(sectors, count, 2, rows, block_size)
    forward = [(cycle[p], cycle[(p + 1) % count]) for p in range(count)]
    backward = [(cycle[p], cycle[(p - 1) % count]) for p in range(count)]
    routes = (forward, backward)
    signs = (1, -1)

    def chunk_id(index):
        return ids[index % count]

    def chunk(half, index):
        picked = lax.dynamic_index_in_dim(blocks, chunk_id(index), 1, keepdims=False)
        return picked[:, half]

    moving = [chunk(h, place - signs[h]) for h in range(2)]
    for step in range(count - 1):
        for h in range(2):
            arrived = lax.ppermute(moving[h], axis, routes[h])
            moving[h] = arrived + chunk(h, place - signs[h] * (step + 2))
    if not gather:
        return jnp.stack(moving, axis=1).reshape(1, sectors, 2 * rows, block_size)
    table = jnp.zeros(blocks.shape, partial.dtype)
    for h in range(2):
        current = moving[h]
        index = place
        table = lax.dynamic_update_slice(
            table, current[:, None, None], (0, chunk_id(index), h, 0, 0)
        )
        for step in range(count - 1):
            current = lax.ppermute(current, axis, routes[h])
            index = place - signs[h] * (step + 1)
            table = lax.dynamic_update_slice(
                table, current[:, None, None], (0, chunk_id(index), h, 0, 0)
            )
    return table.reshape(partial.shape)


def ops_total(value, axis):
    count = lax.axis_size(axis)
    here = lax.axis_index(axis)
    table = jnp.where(jnp.arange(count)[:, None] == here, value[None, :], 0.0)
    for shift in range(1, count):
        sent = lax.ppermute(value, axis, [(i, (i + shift) % count) for i in range(count)])
        table = jnp.where(jnp.arange(count)[:, None] == (here - shift) % count, sent[None, :], table)
    return jnp.sum(table, axis=0)


def gather_sector(values):
    count = lax.axis_size("sector")
    mine = jnp.arange(count)[:, None] == lax.axis_index("sector")
    return lax.psum(jnp.where(mine, values[None, :], 0.0), "sector")


def quotient(vector_wide, sigma_full):
    norm_part = jnp.sum(vector_wide * vector_wide)
    corr_part = jnp.sum(vector_wide * sigma_full)
    local_theta = jnp.where(norm_part > 0, corr_part / jnp.where(norm_part > 0, norm_part, 1.0), 0.0)
    local_rest = sigma_full - local_theta * vector_wide
    rest_part = jnp.sum(local_rest * local_rest)
    cross_part = jnp.sum(vector_wide * local_rest)
    table = gather_sector(jnp.stack([norm_part, corr_part, rest_part, cross_part, local_theta]))
    norms, corrs, rests, crosses, thetas = (table[:, i] for i in range(5))
    rayleigh = jnp.sum(corrs) / jnp.sum(norms)
    shift = thetas - rayleigh
    spread = jnp.sum(rests + 2.0 * shift * crosses + shift * shift * norms)
    return rayleigh, spread


def on_device(psi, left_ops, right_ops, basis, block_dims):
    block_size = psi.shape[2]
    live = live_mask(block_dims, block_size)
    half_env = jnp.einsum(
        "ckqab,cqbd->ckqad", left_ops, basis, preferred_element_type=jnp.float32
    ).astype(jnp.bfloat16)
    boundary_ops = jnp.einsum(
        "cqba,ckqbd->ckqad", basis, half_env, preferred_element_type=jnp.float32
    ).astype(jnp.bfloat16)
    shifted = from_behind(boundary_ops, "chain", 1)
    vector = jnp.where(live > 0, psi, jnp.zeros_like(psi))
    entry_count = float(SECTORS * block_size * block_size)
    share_rows = block_size // lax.axis_size("ops")
    row_start = lax.axis_index("ops") * share_rows
    residual = None
    quotients = []
    for iteration in range(ITERS):
        products = jnp.einsum(
            "ckqab,cqbd->ckqad", shifted, vector, preferred_element_type=jnp.float32
        ).astype(jnp.bfloat16)
        partial_sigma = jnp.einsum(
            "ckqad,ckqed->cqae", products, right_ops, preferred_element_type=jnp.float32
        )
        vector_wide = vector.astype(jnp.float32)
        if iteration + 1 < ITERS:
            sigma_full = ring_sum(partial_sigma, "ops") * live
            rayleigh, spread = quotient(vector_wide, sigma_full)
            quotients.append(rayleigh)
            residue = sigma_full - rayleigh * vector_wide
            vector = (residue * lax.rsqrt(spread / entry_count + 1e-06)).astype(jnp.bfloat16)
        else:
            corr_part = ops_total(jnp.sum(vector_wide * partial_sigma)[None], "ops")[0]
            table = gather_sector(jnp.stack([jnp.sum(vector_wide * vector_wide), corr_part]))
            rayleigh = jnp.sum(table[:, 1]) / jnp.sum(table[:, 0])
            quotients.append(rayleigh)
            sigma_rows = ring_sum(partial_sigma, "ops", gather=False)
            live_rows = lax.dynamic_slice_in_dim(live, row_start, share_rows, 2)
            vector_rows = lax.dynamic_slice_in_dim(vector_wide, row_start, share_rows, 2)
            residual = sigma_rows * live_rows - rayleigh * vector_rows
    thetas = jnp.stack(quotients).reshape(1, ITERS)
    return (residual, thetas)


def solution(mesh):
    in_specs = (
        P("chain", "sector", None, None),
        P("chain", "ops", "sector", None, None),
        P("chain", "ops", "sector", None, None),
        P("chain", "sector", None, None),
        P("chain", "sector"),
    )
    out_specs = (P("chain", "sector", "ops", None), P("chain", None))
    return jax.shard_map(
        on_device, mesh=mesh, in_specs=in_specs, out_specs=out_specs, check_vma=False
    )
```

```python
import jax
import jax.numpy as jnp
from jax import lax
from jax.sharding import PartitionSpec as P

SECTORS = 8
ITERS = 3


def from_behind(block, axis, distance):
    devices = range(lax.axis_size(axis))
    route = [((i - distance) % len(devices), i) for i in devices]
    return lax.ppermute(block, axis, route)


def live_mask(block_dims, block_size):
    index_rows = jnp.arange(block_size, dtype=jnp.int32)
    limits = block_dims[:, :, None, None]
    inside = (index_rows[None, None, :, None] < limits) & (index_rows[None, None, None, :] < limits)
    return inside.astype(jnp.float32)


def ring_order(axis):
    count = lax.axis_size(axis)
    ys = 2
    zs = count // ys
    if count % ys or zs % 2:
        return list(range(count))
    cycle = [z * ys for z in range(zs)]
    for step, z in enumerate(range(zs - 1, -1, -1)):
        cols = range(1, ys) if step % 2 == 0 else range(ys - 1, 0, -1)
        cycle += [z * ys + y for y in cols]
    return cycle


def ring_sum(partial, axis):
    cycle = ring_order(axis)
    count = len(cycle)
    place = jnp.asarray([cycle.index(i) for i in range(count)], jnp.int32)[lax.axis_index(axis)]
    shape = partial.shape
    chunks = partial.reshape(2, count, -1, shape[-1])
    forward = [(cycle[p], cycle[(p + 1) % count]) for p in range(count)]
    backward = [(cycle[p], cycle[(p - 1) % count]) for p in range(count)]
    routes = (forward, backward)
    signs = (1, -1)

    def chunk(half, index):
        return lax.dynamic_index_in_dim(chunks[half], index % count, 0, keepdims=False)

    moving = [chunk(h, place - signs[h]) for h in range(2)]
    for step in range(count - 1):
        for h in range(2):
            arrived = lax.ppermute(moving[h], axis, routes[h])
            moving[h] = arrived + chunk(h, place - signs[h] * (step + 2))
    gathered = []
    for h in range(2):
        table = jnp.zeros(chunks.shape[1:], partial.dtype)
        table = lax.dynamic_update_index_in_dim(table, moving[h], place % count, 0)
        current = moving[h]
        for step in range(count - 1):
            current = lax.ppermute(current, axis, routes[h])
            table = lax.dynamic_update_index_in_dim(
                table, current, (place - signs[h] * (step + 1)) % count, 0
            )
        gathered.append(table)
    return jnp.stack(gathered).reshape(shape)


def gather_sector(values):
    count = lax.axis_size("sector")
    mine = jnp.arange(count)[:, None] == lax.axis_index("sector")
    return lax.psum(jnp.where(mine, values[None, :], 0.0), "sector")


def quotient(vector_wide, sigma_full):
    norm_part = jnp.sum(vector_wide * vector_wide)
    corr_part = jnp.sum(vector_wide * sigma_full)
    local_theta = jnp.where(norm_part > 0, corr_part / jnp.where(norm_part > 0, norm_part, 1.0), 0.0)
    local_rest = sigma_full - local_theta * vector_wide
    rest_part = jnp.sum(local_rest * local_rest)
    cross_part = jnp.sum(vector_wide * local_rest)
    table = gather_sector(jnp.stack([norm_part, corr_part, rest_part, cross_part, local_theta]))
    norms, corrs, rests, crosses, thetas = (table[:, i] for i in range(5))
    rayleigh = jnp.sum(corrs) / jnp.sum(norms)
    shift = thetas - rayleigh
    spread = jnp.sum(rests + 2.0 * shift * crosses + shift * shift * norms)
    return rayleigh, spread


def on_device(psi, left_ops, right_ops, basis, block_dims):
    block_size = psi.shape[2]
    live = live_mask(block_dims, block_size)
    half_env = jnp.einsum(
        "ckqab,cqbd->ckqad", left_ops, basis, preferred_element_type=jnp.float32
    ).astype(jnp.bfloat16)
    boundary_ops = jnp.einsum(
        "cqba,ckqbd->ckqad", basis, half_env, preferred_element_type=jnp.float32
    ).astype(jnp.bfloat16)
    shifted = from_behind(boundary_ops, "chain", 1)
    vector = jnp.where(live > 0, psi, jnp.zeros_like(psi))
    entry_count = float(SECTORS * block_size * block_size)
    share_rows = block_size // lax.axis_size("ops")
    row_start = lax.axis_index("ops") * share_rows
    residual = None
    quotients = []
    for iteration in range(ITERS):
        products = jnp.einsum(
            "ckqab,cqbd->ckqad", shifted, vector, preferred_element_type=jnp.float32
        ).astype(jnp.bfloat16)
        partial_sigma = jnp.einsum(
            "ckqad,ckqed->cqae", products, right_ops, preferred_element_type=jnp.float32
        )
        sigma_full = ring_sum(partial_sigma, "ops") * live
        vector_wide = vector.astype(jnp.float32)
        if iteration + 1 < ITERS:
            rayleigh, spread = quotient(vector_wide, sigma_full)
            quotients.append(rayleigh)
            residue = sigma_full - rayleigh * vector_wide
            vector = (residue * lax.rsqrt(spread / entry_count + 1e-06)).astype(jnp.bfloat16)
        else:
            table = gather_sector(
                jnp.stack([jnp.sum(vector_wide * vector_wide), jnp.sum(vector_wide * sigma_full)])
            )
            rayleigh = jnp.sum(table[:, 1]) / jnp.sum(table[:, 0])
            quotients.append(rayleigh)
            sigma_rows = lax.dynamic_slice_in_dim(sigma_full, row_start, share_rows, 2)
            vector_rows = lax.dynamic_slice_in_dim(vector_wide, row_start, share_rows, 2)
            residual = sigma_rows - rayleigh * vector_rows
    thetas = jnp.stack(quotients).reshape(1, ITERS)
    return (residual, thetas)


def solution(mesh):
    in_specs = (
        P("chain", "sector", None, None),
        P("chain", "ops", "sector", None, None),
        P("chain", "ops", "sector", None, None),
        P("chain", "sector", None, None),
        P("chain", "sector"),
    )
    out_specs = (P("chain", "sector", "ops", None), P("chain", None))
    return jax.shard_map(
        on_device, mesh=mesh, in_specs=in_specs, out_specs=out_specs, check_vma=False
    )
```

```python
import jax
import jax.numpy as jnp
from jax import lax
from jax.sharding import PartitionSpec as P

SECTORS = 8
ITERS = 3


def from_behind(block, axis, distance):
    devices = range(lax.axis_size(axis))
    route = [((i - distance) % len(devices), i) for i in devices]
    return lax.ppermute(block, axis, route)


def live_mask(block_dims, block_size):
    index_rows = jnp.arange(block_size, dtype=jnp.int32)
    limits = block_dims[:, :, None, None]
    inside = (index_rows[None, None, :, None] < limits) & (index_rows[None, None, None, :] < limits)
    return inside.astype(jnp.float32)


def ring_order(axis):
    count = lax.axis_size(axis)
    ys = 2
    zs = count // ys
    if count % ys or zs % 2:
        return list(range(count))
    cycle = [z * ys for z in range(zs)]
    for step, z in enumerate(range(zs - 1, -1, -1)):
        cols = range(1, ys) if step % 2 == 0 else range(ys - 1, 0, -1)
        cycle += [z * ys + y for y in cols]
    return cycle


def ring_sum(partial, axis):
    cycle = ring_order(axis)
    count = len(cycle)
    place = jnp.asarray([cycle.index(i) for i in range(count)], jnp.int32)[lax.axis_index(axis)]
    shape = partial.shape
    chunks = partial.reshape(2, count, -1, shape[-1])
    forward = [(cycle[p], cycle[(p + 1) % count]) for p in range(count)]
    backward = [(cycle[p], cycle[(p - 1) % count]) for p in range(count)]
    routes = (forward, backward)
    signs = (1, -1)

    def chunk(half, index):
        return lax.dynamic_index_in_dim(chunks[half], index % count, 0, keepdims=False)

    moving = [chunk(h, place - signs[h]) for h in range(2)]
    for step in range(count - 1):
        for h in range(2):
            arrived = lax.ppermute(moving[h], axis, routes[h])
            moving[h] = arrived + chunk(h, place - signs[h] * (step + 2))
    gathered = []
    for h in range(2):
        table = jnp.zeros(chunks.shape[1:], partial.dtype)
        table = lax.dynamic_update_index_in_dim(table, moving[h], place % count, 0)
        current = moving[h]
        for step in range(count - 1):
            current = lax.ppermute(current, axis, routes[h])
            table = lax.dynamic_update_index_in_dim(
                table, current, (place - signs[h] * (step + 1)) % count, 0
            )
        gathered.append(table)
    return jnp.stack(gathered).reshape(shape)


def gather_sector(values):
    count = lax.axis_size("sector")
    column = jnp.arange(len(values))
    row = jnp.zeros((len(values),), jnp.float32)
    for index, value in enumerate(values):
        row = jnp.where(column == index, value, row)
    mine = jnp.arange(count)[:, None] == lax.axis_index("sector")
    return lax.psum(jnp.where(mine, row[None, :], 0.0), "sector")


def quotient(vector_wide, sigma_full):
    norm_part = jnp.sum(vector_wide * vector_wide)
    corr_part = jnp.sum(vector_wide * sigma_full)
    local_theta = jnp.where(norm_part > 0, corr_part / jnp.where(norm_part > 0, norm_part, 1.0), 0.0)
    local_rest = sigma_full - local_theta * vector_wide
    rest_part = jnp.sum(local_rest * local_rest)
    cross_part = jnp.sum(vector_wide * local_rest)
    table = gather_sector([norm_part, corr_part, rest_part, cross_part, local_theta])
    norms, corrs, rests, crosses, thetas = (table[:, i] for i in range(5))
    rayleigh = jnp.sum(corrs) / jnp.sum(norms)
    shift = thetas - rayleigh
    spread = jnp.sum(rests + 2.0 * shift * crosses + shift * shift * norms)
    return rayleigh, spread


def on_device(psi, left_ops, right_ops, basis, block_dims):
    block_size = psi.shape[2]
    live = live_mask(block_dims, block_size)
    half_env = jnp.einsum(
        "ckqab,cqbd->ckqad", left_ops, basis, preferred_element_type=jnp.float32
    ).astype(jnp.bfloat16)
    boundary_ops = jnp.einsum(
        "cqba,ckqbd->ckqad", basis, half_env, preferred_element_type=jnp.float32
    ).astype(jnp.bfloat16)
    shifted = from_behind(boundary_ops, "chain", 1)
    vector = jnp.where(live > 0, psi, jnp.zeros_like(psi))
    entry_count = float(SECTORS * block_size * block_size)
    share_rows = block_size // lax.axis_size("ops")
    row_start = lax.axis_index("ops") * share_rows
    residual = None
    quotients = []
    for iteration in range(ITERS):
        products = jnp.einsum(
            "ckqab,cqbd->ckqad", shifted, vector, preferred_element_type=jnp.float32
        ).astype(jnp.bfloat16)
        partial_sigma = jnp.einsum(
            "ckqad,ckqed->cqae", products, right_ops, preferred_element_type=jnp.float32
        )
        sigma_full = ring_sum(partial_sigma, "ops") * live
        vector_wide = vector.astype(jnp.float32)
        if iteration + 1 < ITERS:
            rayleigh, spread = quotient(vector_wide, sigma_full)
            quotients.append(rayleigh)
            residue = sigma_full - rayleigh * vector_wide
            vector = (residue * lax.rsqrt(spread / entry_count + 1e-06)).astype(jnp.bfloat16)
        else:
            table = gather_sector(
                [jnp.sum(vector_wide * vector_wide), jnp.sum(vector_wide * sigma_full)]
            )
            rayleigh = jnp.sum(table[:, 1]) / jnp.sum(table[:, 0])
            quotients.append(rayleigh)
            sigma_rows = lax.dynamic_slice_in_dim(sigma_full, row_start, share_rows, 2)
            vector_rows = lax.dynamic_slice_in_dim(vector_wide, row_start, share_rows, 2)
            residual = sigma_rows - rayleigh * vector_rows
    thetas = jnp.stack(quotients).reshape(1, ITERS)
    return (residual, thetas)


def solution(mesh):
    in_specs = (
        P("chain", "sector", None, None),
        P("chain", "ops", "sector", None, None),
        P("chain", "ops", "sector", None, None),
        P("chain", "sector", None, None),
        P("chain", "sector"),
    )
    out_specs = (P("chain", "sector", "ops", None), P("chain", None))
    return jax.shard_map(
        on_device, mesh=mesh, in_specs=in_specs, out_specs=out_specs, check_vma=False
    )
```

```python
import jax
import jax.numpy as jnp
from jax import lax
from jax.sharding import PartitionSpec as P

SECTORS = 8
ITERS = 3


def from_behind(block, axis, distance):
    devices = range(lax.axis_size(axis))
    route = [((i - distance) % len(devices), i) for i in devices]
    return lax.ppermute(block, axis, route)


def live_mask(block_dims, block_size):
    index_rows = jnp.arange(block_size, dtype=jnp.int32)
    limits = block_dims[:, :, None, None]
    inside = (index_rows[None, None, :, None] < limits) & (index_rows[None, None, None, :] < limits)
    return inside.astype(jnp.float32)


def ring_order(axis):
    count = lax.axis_size(axis)
    ys = 2
    zs = count // ys
    if count % ys or zs % 2:
        return list(range(count))
    cycle = [z * ys for z in range(zs)]
    for step, z in enumerate(range(zs - 1, -1, -1)):
        cols = range(1, ys) if step % 2 == 0 else range(ys - 1, 0, -1)
        cycle += [z * ys + y for y in cols]
    return cycle


def ring_sum(partial, axis):
    cycle = ring_order(axis)
    count = len(cycle)
    place = jnp.asarray([cycle.index(i) for i in range(count)], jnp.int32)[lax.axis_index(axis)]
    shape = partial.shape
    chunks = partial.reshape(2, count, -1, shape[-1])
    forward = [(cycle[p], cycle[(p + 1) % count]) for p in range(count)]
    backward = [(cycle[p], cycle[(p - 1) % count]) for p in range(count)]
    routes = (forward, backward)
    signs = (1, -1)

    def chunk(half, index):
        return lax.dynamic_index_in_dim(chunks[half], index % count, 0, keepdims=False)

    moving = [chunk(h, place - signs[h]) for h in range(2)]
    for step in range(count - 1):
        for h in range(2):
            arrived = lax.ppermute(moving[h], axis, routes[h])
            moving[h] = arrived + chunk(h, place - signs[h] * (step + 2))
    gathered = []
    for h in range(2):
        table = jnp.zeros(chunks.shape[1:], partial.dtype)
        table = lax.dynamic_update_index_in_dim(table, moving[h], place % count, 0)
        current = moving[h]
        for step in range(count - 1):
            current = lax.ppermute(current, axis, routes[h])
            table = lax.dynamic_update_index_in_dim(
                table, current, (place - signs[h] * (step + 1)) % count, 0
            )
        gathered.append(table)
    return jnp.stack(gathered).reshape(shape)


def ring_update(partial, vector, live, entry_count, axis):
    cycle = ring_order(axis)
    count = len(cycle)
    place = jnp.asarray([cycle.index(i) for i in range(count)], jnp.int32)[lax.axis_index(axis)]
    shape = partial.shape
    chunks = partial.reshape(2, count, -1, shape[-1])
    forward = [(cycle[p], cycle[(p + 1) % count]) for p in range(count)]
    backward = [(cycle[p], cycle[(p - 1) % count]) for p in range(count)]
    routes = (forward, backward)
    signs = (1, -1)

    def pick(array, half, index):
        return lax.dynamic_index_in_dim(array.reshape(chunks.shape)[half], index % count, 0, keepdims=False)

    moving = [pick(partial, h, place - signs[h]) for h in range(2)]
    for step in range(count - 1):
        for h in range(2):
            arrived = lax.ppermute(moving[h], axis, routes[h])
            moving[h] = arrived + pick(partial, h, place - signs[h] * (step + 2))
    sigma = jnp.stack(moving) * jnp.stack([pick(live, h, place) for h in range(2)])
    vec = jnp.stack([pick(vector, h, place) for h in range(2)]).astype(jnp.float32)
    norm_part = jnp.sum(vec * vec)
    corr_part = jnp.sum(vec * sigma)
    local_theta = jnp.where(norm_part > 0, corr_part / jnp.where(norm_part > 0, norm_part, 1.0), 0.0)
    local_rest = sigma - local_theta * vec
    values = [norm_part, corr_part, jnp.sum(local_rest * local_rest), jnp.sum(vec * local_rest), local_theta]
    column = jnp.arange(len(values))
    row = jnp.zeros((len(values),), jnp.float32)
    for index, value in enumerate(values):
        row = jnp.where(column == index, value, row)
    here = lax.axis_index(axis)
    table = jnp.where(jnp.arange(count)[:, None] == here, row[None, :], 0.0)
    for shift in range(1, count):
        sent = lax.ppermute(row, axis, [(i, (i + shift) % count) for i in range(count)])
        table = jnp.where(jnp.arange(count)[:, None] == (here - shift) % count, sent[None, :], table)
    table = gather_sector(list(table.reshape(-1))).reshape(-1, len(values))
    norms, corrs, rests, crosses, thetas = (table[:, i] for i in range(len(values)))
    rayleigh = jnp.sum(corrs) / jnp.sum(norms)
    shift = thetas - rayleigh
    spread = jnp.sum(rests + 2.0 * shift * crosses + shift * shift * norms)
    ahead = ((sigma - rayleigh * vec) * lax.rsqrt(spread / entry_count + 1e-06)).astype(jnp.bfloat16)
    gathered = []
    for h in range(2):
        table = jnp.zeros(chunks.shape[1:], jnp.bfloat16)
        table = lax.dynamic_update_index_in_dim(table, ahead[h], place % count, 0)
        current = ahead[h]
        for step in range(count - 1):
            current = lax.ppermute(current, axis, routes[h])
            table = lax.dynamic_update_index_in_dim(
                table, current, (place - signs[h] * (step + 1)) % count, 0
            )
        gathered.append(table)
    return rayleigh, jnp.stack(gathered).reshape(shape)


def gather_sector(values):
    count = lax.axis_size("sector")
    column = jnp.arange(len(values))
    row = jnp.zeros((len(values),), jnp.float32)
    for index, value in enumerate(values):
        row = jnp.where(column == index, value, row)
    mine = jnp.arange(count)[:, None] == lax.axis_index("sector")
    return lax.psum(jnp.where(mine, row[None, :], 0.0), "sector")


def quotient(vector_wide, sigma_full):
    norm_part = jnp.sum(vector_wide * vector_wide)
    corr_part = jnp.sum(vector_wide * sigma_full)
    local_theta = jnp.where(norm_part > 0, corr_part / jnp.where(norm_part > 0, norm_part, 1.0), 0.0)
    local_rest = sigma_full - local_theta * vector_wide
    rest_part = jnp.sum(local_rest * local_rest)
    cross_part = jnp.sum(vector_wide * local_rest)
    table = gather_sector([norm_part, corr_part, rest_part, cross_part, local_theta])
    norms, corrs, rests, crosses, thetas = (table[:, i] for i in range(5))
    rayleigh = jnp.sum(corrs) / jnp.sum(norms)
    shift = thetas - rayleigh
    spread = jnp.sum(rests + 2.0 * shift * crosses + shift * shift * norms)
    return rayleigh, spread


def on_device(psi, left_ops, right_ops, basis, block_dims):
    block_size = psi.shape[2]
    live = live_mask(block_dims, block_size)
    half_env = jnp.einsum(
        "ckqab,cqbd->ckqad", left_ops, basis, preferred_element_type=jnp.float32
    ).astype(jnp.bfloat16)
    boundary_ops = jnp.einsum(
        "cqba,ckqbd->ckqad", basis, half_env, preferred_element_type=jnp.float32
    ).astype(jnp.bfloat16)
    shifted = from_behind(boundary_ops, "chain", 1)
    vector = jnp.where(live > 0, psi, jnp.zeros_like(psi))
    entry_count = float(SECTORS * block_size * block_size)
    share_rows = block_size // lax.axis_size("ops")
    row_start = lax.axis_index("ops") * share_rows
    residual = None
    quotients = []
    for iteration in range(ITERS):
        products = jnp.einsum(
            "ckqab,cqbd->ckqad", shifted, vector, preferred_element_type=jnp.float32
        ).astype(jnp.bfloat16)
        partial_sigma = jnp.einsum(
            "ckqad,ckqed->cqae", products, right_ops, preferred_element_type=jnp.float32
        )
        if iteration + 1 < ITERS:
            rayleigh, vector = ring_update(partial_sigma, vector, live, entry_count, "ops")
            quotients.append(rayleigh)
        else:
            sigma_full = ring_sum(partial_sigma, "ops") * live
            vector_wide = vector.astype(jnp.float32)
            table = gather_sector(
                [jnp.sum(vector_wide * vector_wide), jnp.sum(vector_wide * sigma_full)]
            )
            rayleigh = jnp.sum(table[:, 1]) / jnp.sum(table[:, 0])
            quotients.append(rayleigh)
            sigma_rows = lax.dynamic_slice_in_dim(sigma_full, row_start, share_rows, 2)
            vector_rows = lax.dynamic_slice_in_dim(vector_wide, row_start, share_rows, 2)
            residual = sigma_rows - rayleigh * vector_rows
    thetas = jnp.stack(quotients).reshape(1, ITERS)
    return (residual, thetas)


def solution(mesh):
    in_specs = (
        P("chain", "sector", None, None),
        P("chain", "ops", "sector", None, None),
        P("chain", "ops", "sector", None, None),
        P("chain", "sector", None, None),
        P("chain", "sector"),
    )
    out_specs = (P("chain", "sector", "ops", None), P("chain", None))
    return jax.shard_map(
        on_device, mesh=mesh, in_specs=in_specs, out_specs=out_specs, check_vma=False
    )
```

```python
import jax
import jax.numpy as jnp
from jax import lax
from jax.sharding import PartitionSpec as P

SECTORS = 8
ITERS = 3


def from_behind(block, axis, distance):
    devices = range(lax.axis_size(axis))
    route = [((i - distance) % len(devices), i) for i in devices]
    return lax.ppermute(block, axis, route)


def live_mask(block_dims, block_size):
    index_rows = jnp.arange(block_size, dtype=jnp.int32)
    limits = block_dims[:, :, None, None]
    inside = (index_rows[None, None, :, None] < limits) & (index_rows[None, None, None, :] < limits)
    return inside.astype(jnp.float32)


def ring_order(axis):
    count = lax.axis_size(axis)
    ys = 2
    zs = count // ys
    if count % ys or zs % 2:
        return list(range(count))
    cycle = [z * ys for z in range(zs)]
    for step, z in enumerate(range(zs - 1, -1, -1)):
        cols = range(1, ys) if step % 2 == 0 else range(ys - 1, 0, -1)
        cycle += [z * ys + y for y in cols]
    return cycle


def ring_sum(partial, axis):
    cycle = ring_order(axis)
    count = len(cycle)
    place = jnp.asarray([cycle.index(i) for i in range(count)], jnp.int32)[lax.axis_index(axis)]
    shape = partial.shape
    chunks = partial.reshape(2, count, -1, shape[-1])
    forward = [(cycle[p], cycle[(p + 1) % count]) for p in range(count)]
    backward = [(cycle[p], cycle[(p - 1) % count]) for p in range(count)]
    routes = (forward, backward)
    signs = (1, -1)

    def chunk(half, index):
        return lax.dynamic_index_in_dim(chunks[half], index % count, 0, keepdims=False)

    moving = [chunk(h, place - signs[h]) for h in range(2)]
    for step in range(count - 1):
        for h in range(2):
            arrived = lax.ppermute(moving[h], axis, routes[h])
            moving[h] = arrived + chunk(h, place - signs[h] * (step + 2))
    gathered = []
    for h in range(2):
        table = jnp.zeros(chunks.shape[1:], partial.dtype)
        table = lax.dynamic_update_index_in_dim(table, moving[h], place % count, 0)
        current = moving[h]
        for step in range(count - 1):
            current = lax.ppermute(current, axis, routes[h])
            table = lax.dynamic_update_index_in_dim(
                table, current, (place - signs[h] * (step + 1)) % count, 0
            )
        gathered.append(table)
    return jnp.stack(gathered).reshape(shape)


def gather_sector(values):
    count = lax.axis_size("sector")
    column = jnp.arange(len(values))
    row = jnp.zeros((len(values),), jnp.float32)
    for index, value in enumerate(values):
        row = jnp.where(column == index, value, row)
    mine = jnp.arange(count)[:, None] == lax.axis_index("sector")
    return lax.psum(jnp.where(mine, row[None, :], 0.0), "sector")


def quotient(vector_wide, sigma_full):
    norm_part = jnp.sum(vector_wide * vector_wide)
    corr_part = jnp.sum(vector_wide * sigma_full)
    local_theta = jnp.where(norm_part > 0, corr_part / jnp.where(norm_part > 0, norm_part, 1.0), 0.0)
    local_rest = sigma_full - local_theta * vector_wide
    rest_part = jnp.sum(local_rest * local_rest)
    cross_part = jnp.sum(vector_wide * local_rest)
    table = gather_sector([norm_part, corr_part, rest_part, cross_part, local_theta])
    norms, corrs, rests, crosses, thetas = (table[:, i] for i in range(5))
    rayleigh = jnp.sum(corrs) / jnp.sum(norms)
    shift = thetas - rayleigh
    spread = jnp.sum(rests + 2.0 * shift * crosses + shift * shift * norms)
    return rayleigh, spread


def on_device(psi, left_ops, right_ops, basis, block_dims):
    block_size = psi.shape[2]
    live = live_mask(block_dims, block_size)
    sectors = psi.shape[1]
    cut = sectors // 2 if sectors % 2 == 0 else sectors
    spans = [slice(0, cut)] + ([slice(cut, sectors)] if cut < sectors else [])
    shifted = []
    for span in spans:
        half_env = jnp.einsum(
            "ckqab,cqbd->ckqad", left_ops[:, :, span], basis[:, span], preferred_element_type=jnp.float32
        ).astype(jnp.bfloat16)
        boundary_ops = jnp.einsum(
            "cqba,ckqbd->ckqad", basis[:, span], half_env, preferred_element_type=jnp.float32
        ).astype(jnp.bfloat16)
        shifted.append(from_behind(boundary_ops, "chain", 1))
    vector = jnp.where(live > 0, psi, jnp.zeros_like(psi))
    entry_count = float(SECTORS * block_size * block_size)
    share_rows = block_size // lax.axis_size("ops")
    row_start = lax.axis_index("ops") * share_rows
    residual = None
    quotients = []
    for iteration in range(ITERS):
        pieces = []
        for span, moved in zip(spans, shifted):
            products = jnp.einsum(
                "ckqab,cqbd->ckqad", moved, vector[:, span], preferred_element_type=jnp.float32
            ).astype(jnp.bfloat16)
            pieces.append(jnp.einsum(
                "ckqad,ckqed->cqae", products, right_ops[:, :, span], preferred_element_type=jnp.float32
            ))
        partial_sigma = jnp.concatenate(pieces, axis=1)
        sigma_full = ring_sum(partial_sigma, "ops") * live
        vector_wide = vector.astype(jnp.float32)
        if iteration + 1 < ITERS:
            rayleigh, spread = quotient(vector_wide, sigma_full)
            quotients.append(rayleigh)
            residue = sigma_full - rayleigh * vector_wide
            vector = (residue * lax.rsqrt(spread / entry_count + 1e-06)).astype(jnp.bfloat16)
        else:
            table = gather_sector(
                [jnp.sum(vector_wide * vector_wide), jnp.sum(vector_wide * sigma_full)]
            )
            rayleigh = jnp.sum(table[:, 1]) / jnp.sum(table[:, 0])
            quotients.append(rayleigh)
            sigma_rows = lax.dynamic_slice_in_dim(sigma_full, row_start, share_rows, 2)
            vector_rows = lax.dynamic_slice_in_dim(vector_wide, row_start, share_rows, 2)
            residual = sigma_rows - rayleigh * vector_rows
    thetas = jnp.stack(quotients).reshape(1, ITERS)
    return (residual, thetas)


def solution(mesh):
    in_specs = (
        P("chain", "sector", None, None),
        P("chain", "ops", "sector", None, None),
        P("chain", "ops", "sector", None, None),
        P("chain", "sector", None, None),
        P("chain", "sector"),
    )
    out_specs = (P("chain", "sector", "ops", None), P("chain", None))
    return jax.shard_map(
        on_device, mesh=mesh, in_specs=in_specs, out_specs=out_specs, check_vma=False
    )
```
